256 devices in a mesh: row: 8 (over y, core), col: 16 (over x_lo, z), req: 2 (over x_hi).
Axes of the slice: x: 4 (x_hi: 2, x_lo: 2; x = x_hi * 2 + x_lo), y: 4, z: 8, core: 2. Of those that a mesh axis runs over, the one named last changes fastest.
Arguments:
- tokens: bfloat16 [3072, 4096], P(('req', 'row'), 'col'), may hold values from -6 to 6
- up_weight: bfloat16 [4096, 21504], P('col', 'row'), may hold values from -0.09375 to 0.09375
- down_weight: bfloat16 [21504, 4096], P('row', 'col'), may hold values from -0.0390625 to 0.0390625
- pool_states: float32 [192, 2, 128, 64, 128], P('row', 'req', 'col'), may hold values from -6 to 6
- pool_edges: float32 [192, 2, 128, 64, 3], P('row', 'req', 'col'), may hold values from -6 to 6
- finish_ids: int32 [32], replicated, may hold values from 0 to 191, as said below
- slot_perm: int32 [32], replicated, may hold values from 0 to 31, each once
Outputs:
- layer_out: bfloat16 [3072, 4096], P(('req', 'row'), 'col')
- decode_states: float32 [32, 2, 128, 64, 128], P('req', None, 'col', 'row')
- decode_edges: float32 [32, 2, 128, 64, 3], P('req', None, 'col', 'row')
The draws below stay inside these ranges and needn't reach their ends.
Inputs may be any that keep to these rules, and one draw needn't show every extreme that they name: `finish_ids`: entries are distinct; of the 24 slots r * 24 to (r + 1) * 24 - 1 of one index r of row, at most 8 are named, and exactly 8 for some index. `slot_perm`: every decode slot is named once.
All inputs are finite; a program needn't handle non-finite values.
Results may differ from the reference program's by a relative error of at most 0.0044.
Values may be sent and summed in bfloat16 or wider, within the bound.
No kernel may reach another device: no remote copies, remote signals or barrier semaphores. Data moves between devices by JAX's collectives and lax.ppermute only.
A program may use at most 128 MiB of HBM per device.

```python
import jax
import jax.numpy as jnp
from jax import lax

D = 4096
FF = 21504
H = 128
P_SIZE = 64
N = 128
KW = 3
SLAYERS = 2
TOKENS = 3072
FIN = 32
MOST = 8
POOL_ROW = 24
POOL = 192


def shuffled_slots(one_key):
    return jax.random.permutation(one_key, POOL_ROW).astype(jnp.int32)


def draw_finish_ids(key, part):
    blocks = POOL // POOL_ROW
    key_rows, key_first, key_rank, key_order = jax.random.split(jax.random.fold_in(key, 7), 4)
    row_keys = jax.random.split(key_rows, blocks)
    local_order = jax.vmap(shuffled_slots)(row_keys)[:, :MOST]
    offsets = POOL_ROW * jnp.arange(blocks, dtype=jnp.int32)
    candidates = (local_order + offsets[:, None]).reshape(-1)
    favored = jax.random.randint(key_first, (), 0, blocks)
    ranking = jax.random.permutation(key_rank, blocks * MOST).astype(jnp.int32)
    owners = jnp.arange(blocks * MOST, dtype=jnp.int32) // MOST
    scores = ranking + jnp.where(owners == favored, blocks * MOST, 0).astype(jnp.int32)
    unused, picked = lax.top_k(scores, FIN)
    chosen = candidates[picked]
    shuffle = jax.random.permutation(key_order, FIN)
    return chosen[shuffle].astype(jnp.int32)


def levels(key, extent, cuts, least, top_value):
    level, own = 1.0, jax.random.fold_in(key, 6)
    for axis_at, blocks in cuts:
        draws = jnp.exp(jax.random.uniform(jax.random.fold_in(own, axis_at), (blocks,), jnp.float32, least / len(cuts), top_value / len(cuts)))
        level = level * jnp.repeat(draws, extent[axis_at] // blocks).reshape([-1 if axis == axis_at else 1 for axis in range(len(extent))])
    return level


def normal_values(key, extent, width, bound, cuts=(), kind=jnp.bfloat16):
    gain = levels(key, extent, cuts, -0.22, 0.18) if cuts else 1.0
    drawn = jax.random.normal(key, extent, jnp.float32) * width * gain
    return jnp.minimum(jnp.maximum(drawn, -bound), bound).astype(kind)


def setup_inputs(seed: int = 0) -> dict:
    key_of = jax.random.split(jax.random.key(seed), 8)
    tokens = normal_values(key_of[0], (TOKENS, D), 1.0, 6.0, ((0, 16), (1, 16)))
    up_weight = normal_values(key_of[1], (D, FF), D ** -0.5, 0.09375, ((0, 16), (1, 8)))
    down_weight = normal_values(key_of[2], (FF, D), FF ** -0.5, 0.0390625, ((0, 8), (1, 16)))
    pool_states = normal_values(key_of[3], (POOL, SLAYERS, H, P_SIZE, N), 1.0, 6.0, ((0, 8), (1, 2), (2, 16)), jnp.float32)
    pool_edges = normal_values(key_of[4], (POOL, SLAYERS, H, P_SIZE, KW), 1.0, 6.0, ((0, 8), (1, 2), (2, 16)), jnp.float32)
    finish_ids = draw_finish_ids(jax.random.fold_in(key_of[7], 71), 0)
    slot_perm = jax.random.permutation(key_of[6], FIN).astype(jnp.int32)
    return dict(tokens=tokens, up_weight=up_weight, down_weight=down_weight, pool_states=pool_states, pool_edges=pool_edges, finish_ids=finish_ids, slot_perm=slot_perm)


def reference(tokens, up_weight, down_weight, pool_states, pool_edges, finish_ids, slot_perm):
    preact = jnp.dot(tokens, up_weight, preferred_element_type=jnp.float32)
    active = jnp.maximum(preact, 0.0)
    hidden = (active * active).astype(jnp.bfloat16)
    summed = jnp.dot(hidden, down_weight, preferred_element_type=jnp.float32)
    layer_out = (tokens.astype(jnp.float32) + summed).astype(jnp.bfloat16)
    numbers = jnp.arange(FIN, dtype=jnp.int32)
    matches = slot_perm[None, :] == numbers[:, None]
    source_request = jnp.sum(jnp.where(matches, numbers[None, :], 0), axis=1).astype(jnp.int32)
    source_rows = finish_ids[source_request].astype(jnp.int32)
    return layer_out, pool_states[source_rows], pool_edges[source_rows]
```

```python
import jax
import jax.numpy as jnp
import numpy as np
from jax import lax
from jax.sharding import Mesh
from jax.sharding import PartitionSpec as P

MOST = 8
SWAP = [(0, 1), (1, 0)]


def handover(pool_states, pool_edges, finish_ids, slot_perm):
    local = pool_states.shape[0]
    finished = slot_perm.shape[0]
    r = lax.axis_index("row")
    numbers = jnp.arange(finished, dtype=jnp.int32)
    matches = slot_perm[None, :] == numbers[:, None]
    inverse = jnp.sum(jnp.where(matches, numbers[None, :], 0), axis=1)
    row_of = finish_ids // local
    same = row_of[:, None] == row_of[None, :]
    earlier = numbers[None, :] < numbers[:, None]
    rank = jnp.sum(jnp.where(same & earlier, 1, 0), axis=1)
    slots = jnp.arange(MOST, dtype=jnp.int32)
    chosen = (row_of[None, :] == r) & (rank[None, :] == slots[:, None])
    local_slot = jnp.sum(jnp.where(chosen, finish_ids[None, :] - r * local, 0), axis=1)
    picked = jnp.concatenate([pool_states[local_slot], pool_edges[local_slot]], axis=-1)
    arrived = lax.all_to_all(picked, "row", split_axis=3, concat_axis=0, tiled=True)
    source = inverse
    wanted = row_of[source] * MOST + rank[source]
    rows = arrived[wanted]
    both = lax.all_to_all(rows, "req", split_axis=0, concat_axis=1, tiled=True)
    n = pool_states.shape[-1]
    return both[..., :n], both[..., n:]


def ffn(tokens, up_weight, down_weight):
    i = lax.axis_index("cx")
    block, width = tokens.shape
    half = block // 2
    halves = tokens.reshape(2, half, width)
    mine = lax.dynamic_index_in_dim(halves, i, 0, keepdims=False)
    theirs = lax.dynamic_index_in_dim(halves, 1 - i, 0, keepdims=False)
    recv = lax.ppermute(theirs, "cx", SWAP)
    xa = jnp.concatenate([mine, recv], axis=1)
    xg = lax.all_gather(xa, "row", axis=0, tiled=True)
    w1 = jnp.concatenate([up_weight, lax.ppermute(up_weight, "cx", SWAP)], axis=0)
    preact = lax.psum_scatter(
        jnp.dot(xg, w1, preferred_element_type=jnp.float32),
        "cz",
        scatter_dimension=0,
        tiled=True,
    )
    active = jnp.maximum(preact, 0.0)
    hidden = (active * active).astype(jnp.bfloat16)
    hg = lax.all_gather(hidden, "cz", axis=0, tiled=True)
    w2 = jnp.concatenate([down_weight, lax.ppermute(down_weight, "cx", SWAP)], axis=1)
    products = jnp.dot(hg, w2, preferred_element_type=jnp.float32)
    summed = lax.psum_scatter(products, "row", scatter_dimension=0, tiled=True)
    own = summed[:, :width]
    other = lax.ppermute(summed[:, width:], "cx", SWAP)
    full = jnp.where(i == 0, jnp.concatenate([own, other], 0), jnp.concatenate([other, own], 0))
    return (tokens.astype(jnp.float32) + full).astype(jnp.bfloat16)


def on_device(tokens, up_weight, down_weight, pool_states, pool_edges, finish_ids, slot_perm):
    layer_out = ffn(tokens, up_weight, down_weight)
    decode_states, decode_edges = handover(pool_states, pool_edges, finish_ids, slot_perm)
    return (layer_out, decode_states, decode_edges)


def solution(mesh):
    devices = np.asarray(mesh.devices)
    rows, cols, reqs = devices.shape
    split = Mesh(devices.reshape(rows, 2, cols // 2, reqs), ("row", "cx", "cz", "req"))
    col = ("cx", "cz")
    in_specs = (
        P(("req", "row"), col),
        P(col, "row"),
        P("row", col),
        P("row", "req", col, None, None),
        P("row", "req", col, None, None),
        P(),
        P(),
    )
    out_specs = (
        P(("req", "row"), col),
        P("req", None, col, "row", None),
        P("req", None, col, "row", None),
    )
    return jax.shard_map(
        on_device, mesh=split, in_specs=in_specs, out_specs=out_specs, check_vma=False
    )
```

```python
import jax
import jax.numpy as jnp
import numpy as np
from jax import lax
from jax.sharding import Mesh
from jax.sharding import PartitionSpec as P


MOST = 8
SWAP = [(0, 1), (1, 0)]


def handover(pool_states, pool_edges, finish_ids, slot_perm):
    local = pool_states.shape[0]
    finished = slot_perm.shape[0]
    r = lax.axis_index("row")
    numbers = jnp.arange(finished, dtype=jnp.int32)
    matches = slot_perm[None, :] == numbers[:, None]
    inverse = jnp.sum(jnp.where(matches, numbers[None, :], 0), axis=1)
    row_of = finish_ids // local
    same = row_of[:, None] == row_of[None, :]
    earlier = numbers[None, :] < numbers[:, None]
    rank = jnp.sum(jnp.where(same & earlier, 1, 0), axis=1)
    slots = jnp.arange(MOST, dtype=jnp.int32)
    chosen = (row_of[None, :] == r) & (rank[None, :] == slots[:, None])
    local_slot = jnp.sum(jnp.where(chosen, finish_ids[None, :] - r * local, 0), axis=1)
    picked = jnp.concatenate([pool_states[local_slot], pool_edges[local_slot]], axis=-1)
    arrived = lax.all_to_all(picked, "row", split_axis=3, concat_axis=0, tiled=True)
    wanted = row_of[inverse] * MOST + rank[inverse]
    rows = arrived[wanted]
    both = lax.all_to_all(rows, "req", split_axis=0, concat_axis=1, tiled=True)
    n = pool_states.shape[-1]
    return both[..., :n], both[..., n:]


def ffn(tokens, up_weight, down_weight):
    i = lax.axis_index("cx")
    block, width = tokens.shape
    half = block // 2
    halves = tokens.reshape(2, half, width)
    mine = lax.dynamic_index_in_dim(halves, i, 0, keepdims=False)
    theirs = lax.dynamic_index_in_dim(halves, 1 - i, 0, keepdims=False)
    recv = lax.ppermute(theirs, "cx", SWAP)
    xa = jnp.concatenate([mine, recv], axis=1)
    xg = lax.all_gather(xa, "row", axis=0, tiled=True)
    w1p = lax.ppermute(up_weight, "cx", SWAP)
    w1 = jnp.concatenate([up_weight, w1p], axis=0)
    partial = jnp.dot(xg, w1, preferred_element_type=jnp.float32)
    preact = lax.psum_scatter(partial, "cz", scatter_dimension=0, tiled=True)
    active = jnp.maximum(preact, 0.0)
    hidden = (active * active).astype(jnp.bfloat16)
    hg = lax.all_gather(hidden, "cz", axis=0, tiled=True)
    w2p = lax.ppermute(down_weight, "cx", SWAP)
    w2 = jnp.concatenate([down_weight, w2p], axis=1)
    products = jnp.dot(hg, w2, preferred_element_type=jnp.float32)
    summed = lax.psum_scatter(products, "row", scatter_dimension=0, tiled=True)
    own = summed[:, :width]
    other = lax.ppermute(summed[:, width:], "cx", SWAP)
    full = jnp.where(i == 0, jnp.concatenate([own, other], 0), jnp.concatenate([other, own], 0))
    return (tokens.astype(jnp.float32) + full).astype(jnp.bfloat16)


def on_device(tokens, up_weight, down_weight, pool_states, pool_edges, finish_ids, slot_perm):
    layer_out = ffn(tokens, up_weight, down_weight)
    decode_states, decode_edges = handover(pool_states, pool_edges, finish_ids, slot_perm)
    return (layer_out, decode_states, decode_edges)


def solution(mesh):
    devices = np.asarray(mesh.devices)
    rows, cols, reqs = devices.shape
    split = Mesh(devices.reshape(rows, 2, cols // 2, reqs), ("row", "cx", "cz", "req"))
    col = ("cx", "cz")
    in_specs = (
        P(("req", "row"), col),
        P(col, "row"),
        P("row", col),
        P("row", "req", col, None, None),
        P("row", "req", col, None, None),
        P(),
        P(),
    )
    out_specs = (
        P(("req", "row"), col),
        P("req", None, col, "row", None),
        P("req", None, col, "row", None),
    )
    return jax.shard_map(
        on_device, mesh=split, in_specs=in_specs, out_specs=out_specs, check_vma=False
    )
```

```python
import jax
import jax.numpy as jnp
import numpy as np
from jax import lax
from jax.sharding import Mesh
from jax.sharding import PartitionSpec as P


MOST = 8
SWAP = [(0, 1), (1, 0)]


def handover(pool_states, pool_edges, finish_ids, slot_perm):
    local = pool_states.shape[0]
    finished = slot_perm.shape[0]
    r = lax.axis_index("row")
    numbers = jnp.arange(finished, dtype=jnp.int32)
    matches = slot_perm[None, :] == numbers[:, None]
    inverse = jnp.sum(jnp.where(matches, numbers[None, :], 0), axis=1)
    row_of = finish_ids // local
    same = row_of[:, None] == row_of[None, :]
    earlier = numbers[None, :] < numbers[:, None]
    rank = jnp.sum(jnp.where(same & earlier, 1, 0), axis=1)
    slots = jnp.arange(MOST, dtype=jnp.int32)
    chosen = (row_of[None, :] == r) & (rank[None, :] == slots[:, None])
    local_slot = jnp.sum(jnp.where(chosen, finish_ids[None, :] - r * local, 0), axis=1)
    picked = jnp.concatenate([pool_states[local_slot], pool_edges[local_slot]], axis=-1)
    arrived = lax.all_to_all(picked, "row", split_axis=3, concat_axis=0, tiled=True)
    wanted = row_of[inverse] * MOST + rank[inverse]
    rows = arrived[wanted]
    both = lax.all_to_all(rows, "req", split_axis=0, concat_axis=1, tiled=True)
    n = pool_states.shape[-1]
    return both[..., :n], both[..., n:]


def ffn(tokens, up_weight, down_weight):
    i = lax.axis_index("cx")
    block, width = tokens.shape
    half = block // 2
    halves = tokens.reshape(2, half, width)
    mine = lax.dynamic_index_in_dim(halves, i, 0, keepdims=False)
    theirs = lax.dynamic_index_in_dim(halves, 1 - i, 0, keepdims=False)
    recv = lax.ppermute(theirs, "cx", SWAP)
    xa = jnp.concatenate([mine, recv], axis=1)
    xg = lax.all_gather(xa, "row", axis=0, tiled=True)
    cut = up_weight.shape[1] // 2
    pieces = []
    for w in (up_weight[:, :cut], up_weight[:, cut:]):
        wp = lax.ppermute(w, "cx", SWAP)
        partial = jnp.dot(xg, jnp.concatenate([w, wp], axis=0), preferred_element_type=jnp.float32)
        pieces.append(lax.psum_scatter(partial, "cz", scatter_dimension=0, tiled=True))
    preact = jnp.concatenate(pieces, axis=1)
    active = jnp.maximum(preact, 0.0)
    hidden = (active * active).astype(jnp.bfloat16)
    hg = lax.all_gather(hidden, "cz", axis=0, tiled=True)
    w2p = lax.ppermute(down_weight, "cx", SWAP)
    w2 = jnp.concatenate([down_weight, w2p], axis=1)
    products = jnp.dot(hg, w2, preferred_element_type=jnp.float32)
    summed = lax.psum_scatter(products, "row", scatter_dimension=0, tiled=True)
    own = summed[:, :width]
    other = lax.ppermute(summed[:, width:], "cx", SWAP)
    full = jnp.where(i == 0, jnp.concatenate([own, other], 0), jnp.concatenate([other, own], 0))
    return (tokens.astype(jnp.float32) + full).astype(jnp.bfloat16)


def on_device(tokens, up_weight, down_weight, pool_states, pool_edges, finish_ids, slot_perm):
    layer_out = ffn(tokens, up_weight, down_weight)
    decode_states, decode_edges = handover(pool_states, pool_edges, finish_ids, slot_perm)
    return (layer_out, decode_states, decode_edges)


def solution(mesh):
    devices = np.asarray(mesh.devices)
    rows, cols, reqs = devices.shape
    split = Mesh(devices.reshape(rows, 2, cols // 2, reqs), ("row", "cx", "cz", "req"))
    col = ("cx", "cz")
    in_specs = (
        P(("req", "row"), col),
        P(col, "row"),
        P("row", col),
        P("row", "req", col, None, None),
        P("row", "req", col, None, None),
        P(),
        P(),
    )
    out_specs = (
        P(("req", "row"), col),
        P("req", None, col, "row", None),
        P("req", None, col, "row", None),
    )
    return jax.shard_map(
        on_device, mesh=split, in_specs=in_specs, out_specs=out_specs, check_vma=False
    )
```

```python
import jax
import jax.numpy as jnp
import numpy as np
from jax import lax
from jax.sharding import Mesh
from jax.sharding import PartitionSpec as P


MOST = 8
SWAP = [(0, 1), (1, 0)]
CROSS = [(0, 3), (3, 0), (1, 2), (2, 1)]


def fetch_partner(w, axis):
    cut = w.shape[axis] // 2
    near, far = jnp.split(w, [cut], axis=axis)
    return jnp.concatenate(
        [lax.ppermute(near, "cx", SWAP), lax.ppermute(far, ("cx", "req"), CROSS)], axis=axis
    )


def handover(pool_states, pool_edges, finish_ids, slot_perm):
    local = pool_states.shape[0]
    finished = slot_perm.shape[0]
    r = lax.axis_index("row")
    numbers = jnp.arange(finished, dtype=jnp.int32)
    matches = slot_perm[None, :] == numbers[:, None]
    inverse = jnp.sum(jnp.where(matches, numbers[None, :], 0), axis=1)
    row_of = finish_ids // local
    same = row_of[:, None] == row_of[None, :]
    earlier = numbers[None, :] < numbers[:, None]
    rank = jnp.sum(jnp.where(same & earlier, 1, 0), axis=1)
    slots = jnp.arange(MOST, dtype=jnp.int32)
    chosen = (row_of[None, :] == r) & (rank[None, :] == slots[:, None])
    local_slot = jnp.sum(jnp.where(chosen, finish_ids[None, :] - r * local, 0), axis=1)
    picked = jnp.concatenate([pool_states[local_slot], pool_edges[local_slot]], axis=-1)
    arrived = lax.all_to_all(picked, "row", split_axis=3, concat_axis=0, tiled=True)
    wanted = row_of[inverse] * MOST + rank[inverse]
    rows = arrived[wanted]
    both = lax.all_to_all(rows, "req", split_axis=0, concat_axis=1, tiled=True)
    n = pool_states.shape[-1]
    return both[..., :n], both[..., n:]


def ffn(tokens, up_weight, down_weight):
    i = lax.axis_index("cx")
    block, width = tokens.shape
    half = block // 2
    halves = tokens.reshape(2, half, width)
    mine = lax.dynamic_index_in_dim(halves, i, 0, keepdims=False)
    theirs = lax.dynamic_index_in_dim(halves, 1 - i, 0, keepdims=False)
    recv = lax.ppermute(theirs, "cx", SWAP)
    xa = jnp.concatenate([mine, recv], axis=1)
    xg = lax.all_gather(xa, "row", axis=0, tiled=True)
    w1p = fetch_partner(up_weight, 1)
    w1 = jnp.concatenate([up_weight, w1p], axis=0)
    partial = jnp.dot(xg, w1, preferred_element_type=jnp.float32)
    preact = lax.psum_scatter(partial, "cz", scatter_dimension=0, tiled=True)
    active = jnp.maximum(preact, 0.0)
    hidden = (active * active).astype(jnp.bfloat16)
    hg = lax.all_gather(hidden, "cz", axis=0, tiled=True)
    w2p = fetch_partner(down_weight, 0)
    w2 = jnp.concatenate([down_weight, w2p], axis=1)
    products = jnp.dot(hg, w2, preferred_element_type=jnp.float32)
    summed = lax.psum_scatter(products, "row", scatter_dimension=0, tiled=True)
    own = summed[:, :width]
    other = lax.ppermute(summed[:, width:], "cx", SWAP)
    full = jnp.where(i == 0, jnp.concatenate([own, other], 0), jnp.concatenate([other, own], 0))
    return (tokens.astype(jnp.float32) + full).astype(jnp.bfloat16)


def on_device(tokens, up_weight, down_weight, pool_states, pool_edges, finish_ids, slot_perm):
    layer_out = ffn(tokens, up_weight, down_weight)
    decode_states, decode_edges = handover(pool_states, pool_edges, finish_ids, slot_perm)
    return (layer_out, decode_states, decode_edges)


def solution(mesh):
    devices = np.asarray(mesh.devices)
    rows, cols, reqs = devices.shape
    split = Mesh(devices.reshape(rows, 2, cols // 2, reqs), ("row", "cx", "cz", "req"))
    col = ("cx", "cz")
    in_specs = (
        P(("req", "row"), col),
        P(col, "row"),
        P("row", col),
        P("row", "req", col, None, None),
        P("row", "req", col, None, None),
        P(),
        P(),
    )
    out_specs = (
        P(("req", "row"), col),
        P("req", None, col, "row", None),
        P("req", None, col, "row", None),
    )
    return jax.shard_map(
        on_device, mesh=split, in_specs=in_specs, out_specs=out_specs, check_vma=False
    )
```

```python
import jax
import jax.numpy as jnp
import numpy as np
from jax import lax
from jax.sharding import Mesh
from jax.sharding import PartitionSpec as P


MOST = 8
SWAP = [(0, 1), (1, 0)]
CROSS = [(0, 3), (3, 0), (1, 2), (2, 1)]


def fetch_partner(w, axis):
    cut = w.shape[axis] // 2
    near, far = jnp.split(w, [cut], axis=axis)
    return jnp.concatenate(
        [lax.ppermute(near, "cx", SWAP), lax.ppermute(far, ("cx", "req"), CROSS)], axis=axis
    )


def handover(pool_states, pool_edges, finish_ids, slot_perm):
    local = pool_states.shape[0]
    finished = slot_perm.shape[0]
    r = lax.axis_index("row")
    numbers = jnp.arange(finished, dtype=jnp.int32)
    matches = slot_perm[None, :] == numbers[:, None]
    inverse = jnp.sum(jnp.where(matches, numbers[None, :], 0), axis=1)
    row_of = finish_ids // local
    same = row_of[:, None] == row_of[None, :]
    earlier = numbers[None, :] < numbers[:, None]
    rank = jnp.sum(jnp.where(same & earlier, 1, 0), axis=1)
    slots = jnp.arange(MOST, dtype=jnp.int32)
    chosen = (row_of[None, :] == r) & (rank[None, :] == slots[:, None])
    local_slot = jnp.sum(jnp.where(chosen, finish_ids[None, :] - r * local, 0), axis=1)
    picked = jnp.concatenate([pool_states[local_slot], pool_edges[local_slot]], axis=-1)
    arrived = lax.all_to_all(picked, "row", split_axis=3, concat_axis=0, tiled=True)
    wanted = row_of[inverse] * MOST + rank[inverse]
    rows = arrived[wanted]
    both = lax.all_to_all(rows, "req", split_axis=0, concat_axis=1, tiled=True)
    n = pool_states.shape[-1]
    return both[..., :n], both[..., n:]


def gather_row(x):
    n = lax.axis_size("row")
    r = lax.axis_index("row")
    got = [x] + [
        lax.ppermute(x, "row", [(j, (j + s) % n) for j in range(n)]) for s in range(1, n)
    ]
    ahead = jnp.stack([got[(-t) % n] for t in range(n)])
    return jnp.roll(ahead, r, axis=0).reshape(n * x.shape[0], *x.shape[1:])


def scatter_row(x):
    n = lax.axis_size("row")
    r = lax.axis_index("row")
    blocks = x.reshape(n, x.shape[0] // n, *x.shape[1:])
    total = lax.dynamic_index_in_dim(blocks, r, 0, keepdims=False)
    for s in range(1, n):
        part = lax.dynamic_index_in_dim(blocks, (r + s) % n, 0, keepdims=False)
        total = total + lax.ppermute(part, "row", [(j, (j + s) % n) for j in range(n)])
    return total


def ffn(tokens, up_weight, down_weight):
    i = lax.axis_index("cx")
    block, width = tokens.shape
    half = block // 2
    halves = tokens.reshape(2, half, width)
    mine = lax.dynamic_index_in_dim(halves, i, 0, keepdims=False)
    theirs = lax.dynamic_index_in_dim(halves, 1 - i, 0, keepdims=False)
    recv = lax.ppermute(theirs, "cx", SWAP)
    xa = jnp.concatenate([mine, recv], axis=1)
    xg = gather_row(xa)
    w1p = fetch_partner(up_weight, 1)
    w1 = jnp.concatenate([up_weight, w1p], axis=0)
    partial = jnp.dot(xg, w1, preferred_element_type=jnp.float32)
    preact = lax.psum_scatter(partial, "cz", scatter_dimension=0, tiled=True)
    active = jnp.maximum(preact, 0.0)
    hidden = (active * active).astype(jnp.bfloat16)
    hg = lax.all_gather(hidden, "cz", axis=0, tiled=True)
    w2p = fetch_partner(down_weight, 0)
    w2 = jnp.concatenate([down_weight, w2p], axis=1)
    products = jnp.dot(hg, w2, preferred_element_type=jnp.float32)
    summed = scatter_row(products)
    own = summed[:, :width]
    other = lax.ppermute(summed[:, width:], "cx", SWAP)
    full = jnp.where(i == 0, jnp.concatenate([own, other], 0), jnp.concatenate([other, own], 0))
    return (tokens.astype(jnp.float32) + full).astype(jnp.bfloat16)


def on_device(tokens, up_weight, down_weight, pool_states, pool_edges, finish_ids, slot_perm):
    layer_out = ffn(tokens, up_weight, down_weight)
    decode_states, decode_edges = handover(pool_states, pool_edges, finish_ids, slot_perm)
    return (layer_out, decode_states, decode_edges)


def solution(mesh):
    devices = np.asarray(mesh.devices)
    rows, cols, reqs = devices.shape
    split = Mesh(devices.reshape(rows, 2, cols // 2, reqs), ("row", "cx", "cz", "req"))
    col = ("cx", "cz")
    in_specs = (
        P(("req", "row"), col),
        P(col, "row"),
        P("row", col),
        P("row", "req", col, None, None),
        P("row", "req", col, None, None),
        P(),
        P(),
    )
    out_specs = (
        P(("req", "row"), col),
        P("req", None, col, "row", None),
        P("req", None, col, "row", None),
    )
    return jax.shard_map(
        on_device, mesh=split, in_specs=in_specs, out_specs=out_specs, check_vma=False
    )
```

```python
import jax
import jax.numpy as jnp
import numpy as np
from jax import lax
from jax.sharding import Mesh
from jax.sharding import PartitionSpec as P


MOST = 8
SWAP = [(0, 1), (1, 0)]
CROSS = [(0, 3), (3, 0), (1, 2), (2, 1)]


def fetch_partner(w, axis):
    cut = w.shape[axis] // 2
    near, far = jnp.split(w, [cut], axis=axis)
    return jnp.concatenate(
        [lax.ppermute(near, "cx", SWAP), lax.ppermute(far, ("cx", "req"), CROSS)], axis=axis
    )


def handover(pool_states, pool_edges, finish_ids, slot_perm):
    local = pool_states.shape[0]
    finished = slot_perm.shape[0]
    r = lax.axis_index("row")
    numbers = jnp.arange(finished, dtype=jnp.int32)
    matches = slot_perm[None, :] == numbers[:, None]
    inverse = jnp.sum(jnp.where(matches, numbers[None, :], 0), axis=1)
    row_of = finish_ids // local
    same = row_of[:, None] == row_of[None, :]
    earlier = numbers[None, :] < numbers[:, None]
    rank = jnp.sum(jnp.where(same & earlier, 1, 0), axis=1)
    slots = jnp.arange(MOST, dtype=jnp.int32)
    chosen = (row_of[None, :] == r) & (rank[None, :] == slots[:, None])
    local_slot = jnp.sum(jnp.where(chosen, finish_ids[None, :] - r * local, 0), axis=1)
    picked = jnp.concatenate([pool_states[local_slot], pool_edges[local_slot]], axis=-1)
    arrived = lax.all_to_all(picked, "row", split_axis=3, concat_axis=0, tiled=True)
    wanted = row_of[inverse] * MOST + rank[inverse]
    rows = arrived[wanted]
    both = lax.all_to_all(rows, "req", split_axis=0, concat_axis=1, tiled=True)
    n = pool_states.shape[-1]
    return both[..., :n], both[..., n:]


def down_scatter(hidden, w2):
    n = lax.axis_size("row")
    r = lax.axis_index("row")
    blocks = hidden.reshape(n, hidden.shape[0] // n, hidden.shape[1])

    def part(j):
        block = lax.dynamic_index_in_dim(blocks, j, 0, keepdims=False)
        return jnp.dot(block, w2, preferred_element_type=jnp.float32)

    arrived = [
        lax.ppermute(part((r + s) % n), "row", [(j, (j + s) % n) for j in range(n)])
        for s in range(1, n)
    ]
    total = part(r)
    for piece in arrived:
        total = total + piece
    return total


def ffn(tokens, up_weight, down_weight):
    i = lax.axis_index("cx")
    block, width = tokens.shape
    half = block // 2
    halves = tokens.reshape(2, half, width)
    mine = lax.dynamic_index_in_dim(halves, i, 0, keepdims=False)
    theirs = lax.dynamic_index_in_dim(halves, 1 - i, 0, keepdims=False)
    recv = lax.ppermute(theirs, "cx", SWAP)
    xa = jnp.concatenate([mine, recv], axis=1)
    xg = lax.all_gather(xa, "row", axis=0, tiled=True)
    w1p = fetch_partner(up_weight, 1)
    w1 = jnp.concatenate([up_weight, w1p], axis=0)
    partial = jnp.dot(xg, w1, preferred_element_type=jnp.float32)
    preact = lax.psum_scatter(partial, "cz", scatter_dimension=0, tiled=True)
    active = jnp.maximum(preact, 0.0)
    hidden = (active * active).astype(jnp.bfloat16)
    hg = lax.all_gather(hidden, "cz", axis=0, tiled=True)
    w2p = fetch_partner(down_weight, 0)
    w2 = jnp.concatenate([down_weight, w2p], axis=1)
    summed = down_scatter(hg, w2)
    own = summed[:, :width]
    other = lax.ppermute(summed[:, width:], "cx", SWAP)
    full = jnp.where(i == 0, jnp.concatenate([own, other], 0), jnp.concatenate([other, own], 0))
    return (tokens.astype(jnp.float32) + full).astype(jnp.bfloat16)


def on_device(tokens, up_weight, down_weight, pool_states, pool_edges, finish_ids, slot_perm):
    layer_out = ffn(tokens, up_weight, down_weight)
    decode_states, decode_edges = handover(pool_states, pool_edges, finish_ids, slot_perm)
    return (layer_out, decode_states, decode_edges)


def solution(mesh):
    devices = np.asarray(mesh.devices)
    rows, cols, reqs = devices.shape
    split = Mesh(devices.reshape(rows, 2, cols // 2, reqs), ("row", "cx", "cz", "req"))
    col = ("cx", "cz")
    in_specs = (
        P(("req", "row"), col),
        P(col, "row"),
        P("row", col),
        P("row", "req", col, None, None),
        P("row", "req", col, None, None),
        P(),
        P(),
    )
    out_specs = (
        P(("req", "row"), col),
        P("req", None, col, "row", None),
        P("req", None, col, "row", None),
    )
    return jax.shard_map(
        on_device, mesh=split, in_specs=in_specs, out_specs=out_specs, check_vma=False
    )
```

```python
import jax
import jax.numpy as jnp
import numpy as np
from jax import lax
from jax.sharding import Mesh
from jax.sharding import PartitionSpec as P


MOST = 8
SWAP = [(0, 1), (1, 0)]
CROSS = [(0, 3), (3, 0), (1, 2), (2, 1)]


def fetch_partner(w, axis):
    cut = w.shape[axis] // 2
    near, far = jnp.split(w, [cut], axis=axis)
    return jnp.concatenate(
        [lax.ppermute(near, "cx", SWAP), lax.ppermute(far, ("cx", "req"), CROSS)], axis=axis
    )


def handover(pool_states, pool_edges, finish_ids, slot_perm):
    local = pool_states.shape[0]
    finished = slot_perm.shape[0]
    r = lax.axis_index("row")
    numbers = jnp.arange(finished, dtype=jnp.int32)
    matches = slot_perm[None, :] == numbers[:, None]
    inverse = jnp.sum(jnp.where(matches, numbers[None, :], 0), axis=1)
    row_of = finish_ids // local
    same = row_of[:, None] == row_of[None, :]
    earlier = numbers[None, :] < numbers[:, None]
    rank = jnp.sum(jnp.where(same & earlier, 1, 0), axis=1)
    slots = jnp.arange(MOST, dtype=jnp.int32)
    chosen = (row_of[None, :] == r) & (rank[None, :] == slots[:, None])
    local_slot = jnp.sum(jnp.where(chosen, finish_ids[None, :] - r * local, 0), axis=1)
    picked = jnp.concatenate([pool_states[local_slot], pool_edges[local_slot]], axis=-1)
    arrived = lax.all_to_all(picked, "row", split_axis=3, concat_axis=0, tiled=True)
    wanted = row_of[inverse] * MOST + rank[inverse]
    rows = arrived[wanted]
    both = lax.all_to_all(rows, "req", split_axis=0, concat_axis=1, tiled=True)
    n = pool_states.shape[-1]
    return both[..., :n], both[..., n:]


def scatter_out(x, width):
    rows = lax.axis_size("row")
    n = 2 * rows
    place = lax.axis_index("row") * 2 + lax.axis_index("cx")
    blocks = x.reshape(rows, x.shape[0] // rows, x.shape[1])
    same, other = None, None
    for s in range(n):
        dest = (place + s) % n
        chunk = lax.dynamic_index_in_dim(blocks, dest // 2, 0, keepdims=False)
        chunk = chunk[:, (s % 2) * width:(s % 2 + 1) * width]
        if s:
            chunk = lax.ppermute(chunk, ("row", "cx"), [(j, (j + s) % n) for j in range(n)])
        if s % 2:
            other = chunk if other is None else other + chunk
        else:
            same = chunk if same is None else same + chunk
    return same, other


def ffn(tokens, up_weight, down_weight):
    i = lax.axis_index("cx")
    block, width = tokens.shape
    half = block // 2
    halves = tokens.reshape(2, half, width)
    mine = lax.dynamic_index_in_dim(halves, i, 0, keepdims=False)
    theirs = lax.dynamic_index_in_dim(halves, 1 - i, 0, keepdims=False)
    recv = lax.ppermute(theirs, "cx", SWAP)
    xa = jnp.concatenate([mine, recv], axis=1)
    xg = lax.all_gather(xa, "row", axis=0, tiled=True)
    w1p = fetch_partner(up_weight, 1)
    w1 = jnp.concatenate([up_weight, w1p], axis=0)
    partial = jnp.dot(xg, w1, preferred_element_type=jnp.float32)
    preact = lax.psum_scatter(partial, "cz", scatter_dimension=0, tiled=True)
    active = jnp.maximum(preact, 0.0)
    hidden = (active * active).astype(jnp.bfloat16)
    hg = lax.all_gather(hidden, "cz", axis=0, tiled=True)
    w2p = fetch_partner(down_weight, 0)
    w2 = jnp.concatenate([down_weight, w2p], axis=1)
    products = jnp.dot(hg, w2, preferred_element_type=jnp.float32)
    own, other = scatter_out(products, width)
    full = jnp.where(i == 0, jnp.concatenate([own, other], 0), jnp.concatenate([other, own], 0))
    return (tokens.astype(jnp.float32) + full).astype(jnp.bfloat16)


def on_device(tokens, up_weight, down_weight, pool_states, pool_edges, finish_ids, slot_perm):
    layer_out = ffn(tokens, up_weight, down_weight)
    decode_states, decode_edges = handover(pool_states, pool_edges, finish_ids, slot_perm)
    return (layer_out, decode_states, decode_edges)


def solution(mesh):
    devices = np.asarray(mesh.devices)
    rows, cols, reqs = devices.shape
    split = Mesh(devices.reshape(rows, 2, cols // 2, reqs), ("row", "cx", "cz", "req"))
    col = ("cx", "cz")
    in_specs = (
        P(("req", "row"), col),
        P(col, "row"),
        P("row", col),
        P("row", "req", col, None, None),
        P("row", "req", col, None, None),
        P(),
        P(),
    )
    out_specs = (
        P(("req", "row"), col),
        P("req", None, col, "row", None),
        P("req", None, col, "row", None),
    )
    return jax.shard_map(
        on_device, mesh=split, in_specs=in_specs, out_specs=out_specs, check_vma=False
    )
```

```python
import jax
import jax.numpy as jnp
import numpy as np
from jax import lax
from jax.sharding import Mesh
from jax.sharding import PartitionSpec as P


MOST = 8
SWAP = [(0, 1), (1, 0)]
CROSS = [(0, 3), (3, 0), (1, 2), (2, 1)]


def fetch_partner(w, axis):
    cut = w.shape[axis] // 2
    near, far = jnp.split(w, [cut], axis=axis)
    return jnp.concatenate(
        [lax.ppermute(near, "cx", SWAP), lax.ppermute(far, ("cx", "req"), CROSS)], axis=axis
    )


def handover(pool_states, pool_edges, finish_ids, slot_perm):
    local = pool_states.shape[0]
    finished = slot_perm.shape[0]
    r = lax.axis_index("row")
    numbers = jnp.arange(finished, dtype=jnp.int32)
    matches = slot_perm[None, :] == numbers[:, None]
    inverse = jnp.sum(jnp.where(matches, numbers[None, :], 0), axis=1)
    row_of = finish_ids // local
    same = row_of[:, None] == row_of[None, :]
    earlier = numbers[None, :] < numbers[:, None]
    rank = jnp.sum(jnp.where(same & earlier, 1, 0), axis=1)
    slots = jnp.arange(MOST, dtype=jnp.int32)
    chosen = (row_of[None, :] == r) & (rank[None, :] == slots[:, None])
    local_slot = jnp.sum(jnp.where(chosen, finish_ids[None, :] - r * local, 0), axis=1)
    picked = jnp.concatenate([pool_states[local_slot], pool_edges[local_slot]], axis=-1)
    arrived = lax.all_to_all(picked, "row", split_axis=3, concat_axis=0, tiled=True)
    wanted = row_of[inverse] * MOST + rank[inverse]
    rows = arrived[wanted]
    both = lax.all_to_all(rows, "req", split_axis=0, concat_axis=1, tiled=True)
    n = pool_states.shape[-1]
    return both[..., :n], both[..., n:]


def scatter_row(x):
    n = lax.axis_size("row")
    r = lax.axis_index("row")
    blocks = x.reshape(n, x.shape[0] // n, *x.shape[1:])
    total = lax.dynamic_index_in_dim(blocks, r, 0, keepdims=False)
    for s in sorted(range(1, n), key=lambda s: -min(s, n - s)):
        part = lax.dynamic_index_in_dim(blocks, (r + s) % n, 0, keepdims=False)
        total = total + lax.ppermute(part, "row", [(j, (j + s) % n) for j in range(n)])
    return total


def ffn(tokens, up_weight, down_weight):
    i = lax.axis_index("cx")
    block, width = tokens.shape
    half = block // 2
    halves = tokens.reshape(2, half, width)
    mine = lax.dynamic_index_in_dim(halves, i, 0, keepdims=False)
    theirs = lax.dynamic_index_in_dim(halves, 1 - i, 0, keepdims=False)
    recv = lax.ppermute(theirs, "cx", SWAP)
    xa = jnp.concatenate([mine, recv], axis=1)
    xg = lax.all_gather(xa, "row", axis=0, tiled=True)
    w1p = fetch_partner(up_weight, 1)
    w1 = jnp.concatenate([up_weight, w1p], axis=0)
    partial = jnp.dot(xg, w1, preferred_element_type=jnp.float32)
    preact = lax.psum_scatter(partial, "cz", scatter_dimension=0, tiled=True)
    active = jnp.maximum(preact, 0.0)
    hidden = (active * active).astype(jnp.bfloat16)
    hg = lax.all_gather(hidden, "cz", axis=0, tiled=True)
    w2p = fetch_partner(down_weight, 0)
    w2 = jnp.concatenate([down_weight, w2p], axis=1)
    products = jnp.dot(hg, w2, preferred_element_type=jnp.float32)
    summed = scatter_row(products)
    own = summed[:, :width]
    other = lax.ppermute(summed[:, width:], "cx", SWAP)
    full = jnp.where(i == 0, jnp.concatenate([own, other], 0), jnp.concatenate([other, own], 0))
    return (tokens.astype(jnp.float32) + full).astype(jnp.bfloat16)


def on_device(tokens, up_weight, down_weight, pool_states, pool_edges, finish_ids, slot_perm):
    layer_out = ffn(tokens, up_weight, down_weight)
    decode_states, decode_edges = handover(pool_states, pool_edges, finish_ids, slot_perm)
    return (layer_out, decode_states, decode_edges)


def solution(mesh):
    devices = np.asarray(mesh.devices)
    rows, cols, reqs = devices.shape
    split = Mesh(devices.reshape(rows, 2, cols // 2, reqs), ("row", "cx", "cz", "req"))
    col = ("cx", "cz")
    in_specs = (
        P(("req", "row"), col),
        P(col, "row"),
        P("row", col),
        P("row", "req", col, None, None),
        P("row", "req", col, None, None),
        P(),
        P(),
    )
    out_specs = (
        P(("req", "row"), col),
        P("req", None, col, "row", None),
        P("req", None, col, "row", None),
    )
    return jax.shard_map(
        on_device, mesh=split, in_specs=in_specs, out_specs=out_specs, check_vma=False
    )
```

```python
import jax
import jax.numpy as jnp
import numpy as np
from jax import lax
from jax.sharding import Mesh
from jax.sharding import PartitionSpec as P


MOST = 8
SWAP = [(0, 1), (1, 0)]
CROSS = [(0, 3), (3, 0), (1, 2), (2, 1)]


def fetch_partner(w, axis):
    cut = w.shape[axis] // 2
    near, far = jnp.split(w, [cut], axis=axis)
    return jnp.concatenate(
        [lax.ppermute(near, "cx", SWAP), lax.ppermute(far, ("cx", "req"), CROSS)], axis=axis
    )


def handover(pool_states, pool_edges, finish_ids, slot_perm):
    local = pool_states.shape[0]
    finished = slot_perm.shape[0]
    r = lax.axis_index("row")
    numbers = jnp.arange(finished, dtype=jnp.int32)
    matches = slot_perm[None, :] == numbers[:, None]
    inverse = jnp.sum(jnp.where(matches, numbers[None, :], 0), axis=1)
    row_of = finish_ids // local
    same = row_of[:, None] == row_of[None, :]
    earlier = numbers[None, :] < numbers[:, None]
    rank = jnp.sum(jnp.where(same & earlier, 1, 0), axis=1)
    slots = jnp.arange(MOST, dtype=jnp.int32)
    chosen = (row_of[None, :] == r) & (rank[None, :] == slots[:, None])
    local_slot = jnp.sum(jnp.where(chosen, finish_ids[None, :] - r * local, 0), axis=1)
    picked = jnp.concatenate([pool_states[local_slot], pool_edges[local_slot]], axis=-1)
    arrived = lax.all_to_all(picked, "row", split_axis=3, concat_axis=0, tiled=True)
    wanted = row_of[inverse] * MOST + rank[inverse]
    rows = arrived[wanted]
    both = lax.all_to_all(rows, "req", split_axis=0, concat_axis=1, tiled=True)
    n = pool_states.shape[-1]
    return both[..., :n], both[..., n:]


def scatter_row(x):
    n = lax.axis_size("row")
    r = lax.axis_index("row")
    blocks = x.reshape(n, x.shape[0] // n, *x.shape[1:])
    pieces = [lax.dynamic_index_in_dim(blocks, r, 0, keepdims=False)]
    for s in sorted(range(1, n), key=lambda s: -min(s, n - s)):
        part = lax.dynamic_index_in_dim(blocks, (r + s) % n, 0, keepdims=False)
        pieces.append(lax.ppermute(part, "row", [(j, (j + s) % n) for j in range(n)]))
    return pieces


def ffn(tokens, up_weight, down_weight):
    i = lax.axis_index("cx")
    block, width = tokens.shape
    half = block // 2
    halves = tokens.reshape(2, half, width)
    mine = lax.dynamic_index_in_dim(halves, i, 0, keepdims=False)
    theirs = lax.dynamic_index_in_dim(halves, 1 - i, 0, keepdims=False)
    recv = lax.ppermute(theirs, "cx", SWAP)
    xa = jnp.concatenate([mine, recv], axis=1)
    xg = lax.all_gather(xa, "row", axis=0, tiled=True)
    w1p = fetch_partner(up_weight, 1)
    w1 = jnp.concatenate([up_weight, w1p], axis=0)
    partial = jnp.dot(xg, w1, preferred_element_type=jnp.float32)
    preact = lax.psum_scatter(partial, "cz", scatter_dimension=0, tiled=True)
    active = jnp.maximum(preact, 0.0)
    hidden = (active * active).astype(jnp.bfloat16)
    hg = lax.all_gather(hidden, "cz", axis=0, tiled=True)
    w2p = fetch_partner(down_weight, 0)
    w2 = jnp.concatenate([down_weight, w2p], axis=1)
    products = jnp.dot(hg, w2, preferred_element_type=jnp.float32)
    pieces = scatter_row(products)
    other = lax.ppermute(sum(p[:, width:] for p in pieces), "cx", SWAP)
    own = sum(p[:, :width] for p in pieces)
    full = jnp.where(i == 0, jnp.concatenate([own, other], 0), jnp.concatenate([other, own], 0))
    return (tokens.astype(jnp.float32) + full).astype(jnp.bfloat16)


def on_device(tokens, up_weight, down_weight, pool_states, pool_edges, finish_ids, slot_perm):
    layer_out = ffn(tokens, up_weight, down_weight)
    decode_states, decode_edges = handover(pool_states, pool_edges, finish_ids, slot_perm)
    return (layer_out, decode_states, decode_edges)


def solution(mesh):
    devices = np.asarray(mesh.devices)
    rows, cols, reqs = devices.shape
    split = Mesh(devices.reshape(rows, 2, cols // 2, reqs), ("row", "cx", "cz", "req"))
    col = ("cx", "cz")
    in_specs = (
        P(("req", "row"), col),
        P(col, "row"),
        P("row", col),
        P("row", "req", col, None, None),
        P("row", "req", col, None, None),
        P(),
        P(),
    )
    out_specs = (
        P(("req", "row"), col),
        P("req", None, col, "row", None),
        P("req", None, col, "row", None),
    )
    return jax.shard_map(
        on_device, mesh=split, in_specs=in_specs, out_specs=out_specs, check_vma=False
    )
```
